512 devices in a mesh: grp: 16 (over y, core), dom: 32 (over x, z).
Axes of the slice: x: 4, y: 8, z: 8, core: 2. Of those that a mesh axis runs over, the one named last changes fastest.
Arguments:
- owned_blips: bfloat16 [2048, 32768], P(('grp', 'dom')), may hold values from -6 to 6
- potential: float32 [32, 512, 1024], P('dom', 'grp'), may hold values from -5 to 5
- slot_owner: int32 [12288, 1], P(('grp', 'dom')), may hold values from 0 to 31; in each aligned block of 24 rows (0 to 23, 24 to 47, ...) at most 2 rows name the same one
- slot_row: int32 [12288], P(('grp', 'dom')), may hold values from 0 to 3
- slot_offset: int32 [12288], P(('grp', 'dom')), may hold values from 0 to 31
Outputs:
- blip_gradient: float32 [2048, 32768], P(('grp', 'dom'))
- hamiltonian: float32 [2048, 128], P(('grp', 'dom'))
The draws below stay inside these ranges and needn't reach their ends.
Inputs may be any that keep to these rules, and one draw needn't show every extreme that they name: `slot_owner`: among the 24 pieces of one device at most 2 name the same owner.
All inputs are finite; a program needn't handle non-finite values.
Results may differ from the reference program's by a relative error of at most 0.012.
The reference program's roundings to bfloat16 on the way (of `slot_blips`, `back_plane` and `gradient_piece`) count: a program that leaves them out, or rounds other values in their place, can miss the bound.
Values may be sent and summed in bfloat16 or wider, within the bound.
No kernel may reach another device: no remote copies, remote signals or barrier semaphores. Data moves between devices by JAX's collectives and lax.ppermute only.
A program may use at most 128 MiB of HBM per device.

```python
import math
import jax
import jax.numpy as jnp
import numpy as np
from jax import lax

NB = 32
S_DEV = 4
SLOTS = 24
PY = 32
NN = 1024
NB3 = 32768
CAP = 2
SUPPORTS = 2048
N_GRP = 16
N_DOM = 32


def set_ends(entries, stream_key, low, high):
    spot = [jax.random.randint(jax.random.fold_in(stream_key, axis), (), 0, length) for axis, length in enumerate(entries.shape)]
    widest = entries.shape.index(max(entries.shape))
    next_to = spot[:widest] + [(spot[widest] + 1) % entries.shape[widest]] + spot[widest + 1:]
    return entries.at[tuple(spot)].set(low).at[tuple(next_to)].set(high)


def levels(rng, extent, split, smallest, high):
    loudness = 1.0
    for position, parts in split:
        heights = jax.random.uniform(jax.random.fold_in(jax.random.fold_in(rng, 6), position), (parts,), jnp.float32, smallest / len(split), high / len(split))
        loudness = loudness * jnp.repeat(jnp.exp(heights), extent[position] // parts).reshape((-1,) + (1,) * (len(extent) - 1 - position))
    return loudness


def deal_out(key, own, number, rows, number_of, top, most, lean):
    ranking = jax.random.permutation(key, number_of)
    heavy_load, usual = portions_of(number_of, rows * top, most, lean, True), portions_of(number_of, rows * top, most, lean, False)
    places = jnp.arange(number_of)

    def named(tallies, offset_by):
        used = int((tallies > 0).sum())
        fixed = max(1, used // 4)
        moved = fixed + (places - fixed + offset_by * (used - fixed)) % max(1, number_of - fixed)
        return jnp.zeros((number_of,), jnp.int32).at[ranking[jnp.where(places < fixed, places, moved)]].set(jnp.asarray(tallies, jnp.int32))

    tallies = jnp.where(number % 4 == 0, named(heavy_load, number // 4), named(usual, number - number // 4 - 1))
    mixed = jax.random.permutation(jax.random.fold_in(own, 3), number_of)
    giver, taker = mixed[0:number_of // 2 * 2:2], mixed[1:number_of // 2 * 2:2]
    room = jnp.minimum(tallies[giver] - 1, most - tallies[taker]) // 2
    room = jnp.where((giver == ranking[0]) | (taker == ranking[0]) | (tallies[taker] == 0), 0, jnp.maximum(room, 0))
    moved = jax.random.randint(jax.random.fold_in(own, 4), (number_of // 2,), 0, 1 << 20) % (room + 1)
    tallies = tallies.at[giver].add(-moved).at[taker].add(moved)
    members = jnp.searchsorted(jnp.cumsum(tallies), jnp.arange(rows * top), side="right").astype(jnp.int32)
    grid = members.reshape(top, rows).T
    grid = grid[jax.random.permutation(jax.random.fold_in(own, 1), rows)]
    offset_by = jax.random.randint(jax.random.fold_in(own, 2), (rows, 1), 0, top)
    return jnp.take_along_axis(grid, (jnp.arange(top)[None, :] + offset_by) % top, axis=1)


def portions_of(amount, total, bound, lean, full):
    portions = [(1 << 20) // math.isqrt(grade ** lean) + 1 for grade in range(1, amount + 1)]
    largest = bound if full else min(bound, max(-(-total // amount), total * portions[0] // sum(portions)))
    least = 1 if total - largest >= amount - 1 else 0
    counts, surplus = [largest] + [least] * (amount - 1), total - largest - least * (amount - 1)
    while surplus > 0:
        candidates = [i for i in range(1, amount) if counts[i] < largest] or [i for i in range(1, amount) if counts[i] < bound]
        pool, budget = sum([portions[i] for i in candidates]), surplus
        for i in candidates:
            more = min(bound - counts[i], max(1, budget * portions[i] // pool), surplus)
            counts[i] = counts[i] + more
            surplus = surplus - more
    return np.array(counts)


def bell_draw(own_key, dims, scale, bound, cuts=(), kind=jnp.bfloat16):
    gain = levels(own_key, dims, cuts, -0.22, 0.18) if cuts else 1.0
    drawn = jax.random.normal(own_key, dims, jnp.float32) * scale * gain
    return jnp.minimum(jnp.maximum(drawn, -bound), bound).astype(kind)


def setup_inputs(seed: int = 0) -> dict:
    seeds = jax.random.split(jax.random.key(seed), 6)
    owned_blips = bell_draw(seeds[0], (SUPPORTS, NB3), 1.0, 6.0, ((0, 512),))
    potential = bell_draw(seeds[1], (N_DOM, N_GRP * PY, NN), 1.0, 5.0, ((0, 32), (1, 16)), jnp.float32)
    slot_owner_keys = jax.random.split(jax.random.fold_in(seeds[2], 1), (N_GRP * N_DOM * SLOTS) // SLOTS)
    slot_owner_turns = jax.random.permutation(jax.random.fold_in(seeds[2], 3), (N_GRP * N_DOM * SLOTS) // SLOTS)
    slot_owner = jax.vmap(lambda own, number: deal_out(jax.random.fold_in(seeds[2], 2), own, number, SLOTS, N_DOM, 1, CAP, 2))(slot_owner_keys, slot_owner_turns).reshape((N_GRP * N_DOM * SLOTS, 1))
    slot_row = set_ends(jax.random.randint(seeds[3], (N_GRP * N_DOM * SLOTS,), 0, S_DEV), jax.random.fold_in(seeds[3], 1), 0, S_DEV - 1).astype(jnp.int32)
    slot_offset = set_ends(jax.random.randint(seeds[4], (N_GRP * N_DOM * SLOTS,), 0, PY), jax.random.fold_in(seeds[4], 1), 0, PY - 1).astype(jnp.int32)
    return dict(owned_blips=owned_blips, potential=potential, slot_owner=slot_owner, slot_row=slot_row, slot_offset=slot_offset)


def spline_tables():
    cells_line = jnp.arange(NB, dtype=jnp.int32)
    offset = cells_line[:, None] - cells_line[None, :]
    spline = jnp.where(offset == 0, 2.0 / 3.0, jnp.where(jnp.abs(offset) == 1, 1.0 / 6.0, 0.0)).astype(jnp.float32)
    second = jnp.where(offset == 0, -2.0, jnp.where(jnp.abs(offset) == 1, 1.0, 0.0)).astype(jnp.float32)
    plane_value = jnp.einsum("ac,bd->abcd", spline, spline).reshape(NB * NB, NB * NB)
    plane_curve = (jnp.einsum("ac,bd->abcd", second, spline) + jnp.einsum("ac,bd->abcd", spline, second)).reshape(NB * NB, NB * NB)
    return (spline.astype(jnp.bfloat16), second.astype(jnp.bfloat16), plane_value.astype(jnp.bfloat16), plane_curve.astype(jnp.bfloat16))


def domain_terms(slot_blips, window, tables):
    spline, second, plane_value, plane_curve = [table.astype(jnp.float32) for table in tables]
    highest = lax.Precision.HIGHEST
    count_slots = slot_blips.shape[0]
    layered = slot_blips.reshape(count_slots, NB, NB * NB).astype(jnp.float32)
    y_value = jnp.einsum("ya,sab->syb", spline, layered, precision=highest).astype(jnp.bfloat16).astype(jnp.float32)
    y_curve = jnp.einsum("ya,sab->syb", second, layered, precision=highest).astype(jnp.bfloat16).astype(jnp.float32)
    values_grid = jnp.einsum("syb,bc->syc", y_value, plane_value, precision=highest)
    laplace = jnp.einsum("syb,bc->syc", y_curve, plane_value, precision=highest) + jnp.einsum("syb,bc->syc", y_value, plane_curve, precision=highest)
    applied = (-0.5 * laplace + window * values_grid).astype(jnp.bfloat16).astype(jnp.float32)
    values_low = values_grid.astype(jnp.bfloat16).astype(jnp.float32)
    back_plane = jnp.einsum("syb,bc->syc", applied, plane_value, precision=highest).astype(jnp.bfloat16).astype(jnp.float32)
    gradient_piece = jnp.einsum("ay,sab->syb", spline, back_plane, precision=highest).astype(jnp.bfloat16)
    intersection = jnp.einsum("sk,tk->st", values_low.reshape(count_slots, -1), applied.reshape(count_slots, -1), precision=highest) / float(NB * NB * NB)
    return gradient_piece.reshape(count_slots, NB * NB * NB), intersection


def reference(owned_blips, potential, slot_owner, slot_row, slot_offset):
    tables = spline_tables()
    group_blips = owned_blips.reshape(N_GRP, N_DOM * S_DEV, NB * NB * NB)
    owners = slot_owner.reshape(N_GRP, N_DOM, SLOTS).astype(jnp.int32)
    targets = owners * S_DEV + slot_row.reshape(N_GRP, N_DOM, SLOTS).astype(jnp.int32)
    offsets = slot_offset.reshape(N_GRP, N_DOM, SLOTS).astype(jnp.int32)
    columns = jnp.arange(N_DOM * S_DEV, dtype=jnp.int32)

    def one_domain(state_pair, domain_index):
        gradient, hamilton = state_pair
        group_index = (domain_index // N_DOM).astype(jnp.int32)
        domain = (domain_index % N_DOM).astype(jnp.int32)
        target = targets[group_index, domain]
        slot_blips = group_blips[group_index][target]
        field = potential[domain]
        lower_cells = lax.dynamic_slice_in_dim(field, (group_index * PY).astype(jnp.int32), PY, 0)
        upper_cells = lax.dynamic_slice_in_dim(field, (((group_index + 1) % N_GRP) * PY).astype(jnp.int32), PY, 0)
        extended = jnp.concatenate([lower_cells, upper_cells], axis=0)

        def cut_window(first_row):
            return lax.dynamic_slice_in_dim(extended, first_row, NB, 0)

        window = jax.vmap(cut_window)(offsets[group_index, domain])
        gradient_piece, intersection = domain_terms(slot_blips, window, tables)
        gradient = gradient.at[group_index, target].add(gradient_piece.astype(jnp.float32))
        select = (target[:, None] == columns[None, :]).astype(jnp.float32)
        weighted = jnp.dot(intersection, select, precision=lax.Precision.HIGHEST)
        hamilton = hamilton.at[group_index].add(jnp.dot(select.T, weighted, precision=lax.Precision.HIGHEST))
        return (gradient, hamilton), None

    start_state = (jnp.zeros((N_GRP, N_DOM * S_DEV, NB * NB * NB), jnp.float32), jnp.zeros((N_GRP, N_DOM * S_DEV, N_DOM * S_DEV), jnp.float32))
    final_state, unused = lax.scan(one_domain, start_state, jnp.arange(N_GRP * N_DOM, dtype=jnp.int32))
    gradient, hamilton = final_state
    return (gradient.reshape(N_GRP * N_DOM * S_DEV, NB * NB * NB), hamilton.reshape(N_GRP * N_DOM * S_DEV, N_DOM * S_DEV))
```

```python
import jax
import jax.numpy as jnp
from jax import lax
from jax.sharding import PartitionSpec as P

NB = 32


def passed_along(block, axis, distance):
    devices = range(lax.axis_size(axis))
    route = [((i - distance) % len(devices), i) for i in devices]
    return lax.ppermute(block, axis, route)


def spline_tables():
    cells_line = jnp.arange(NB, dtype=jnp.int32)
    offset = cells_line[:, None] - cells_line[None, :]
    spline = jnp.where(
        offset == 0, 2.0 / 3.0, jnp.where(jnp.abs(offset) == 1, 1.0 / 6.0, 0.0)
    ).astype(jnp.float32)
    second = jnp.where(offset == 0, -2.0, jnp.where(jnp.abs(offset) == 1, 1.0, 0.0)).astype(
        jnp.float32
    )
    plane_value = jnp.einsum("ac,bd->abcd", spline, spline).reshape(NB * NB, NB * NB)
    plane_curve = (
        jnp.einsum("ac,bd->abcd", second, spline) + jnp.einsum("ac,bd->abcd", spline, second)
    ).reshape(NB * NB, NB * NB)
    return (
        spline.astype(jnp.bfloat16),
        second.astype(jnp.bfloat16),
        plane_value.astype(jnp.bfloat16),
        plane_curve.astype(jnp.bfloat16),
    )


def on_device(owned_blips, potential, slot_owner, slot_row, slot_offset):
    spline, second, plane_value, plane_curve = spline_tables()
    domain_count = lax.axis_size("dom")
    slot_count = slot_row.shape[0]
    owned_count = owned_blips.shape[0]
    cell_count = owned_blips.shape[1]
    plane_cells = NB * NB
    capacity = max(2, -(-slot_count // domain_count))
    group_size = domain_count * owned_count
    owner_of = slot_owner[:, 0]
    target = owner_of * owned_count + slot_row
    owner_hot = (owner_of[:, None] == jnp.arange(domain_count, dtype=jnp.int32)[None, :]).astype(
        jnp.int32
    )
    position = jnp.sum(jnp.cumsum(owner_hot, axis=0) * owner_hot, axis=1) - 1
    place_slot = owner_of * capacity + position
    place_hot = place_slot[None, :] == jnp.arange(domain_count * capacity, dtype=jnp.int32)[:, None]
    asked_rows = jnp.sum(jnp.where(place_hot, slot_row[None, :], 0), axis=1) + owned_count * (
        1 - jnp.sum(place_hot.astype(jnp.int32), axis=1)
    )
    place_low = place_hot.astype(jnp.bfloat16)
    gathered_rows = lax.all_gather(owned_blips, "dom", axis=0, tiled=True)
    chosen = (
        target[:, None] == jnp.arange(gathered_rows.shape[0], dtype=jnp.int32)[None, :]
    ).astype(jnp.bfloat16)
    slot_blips = jnp.dot(chosen, gathered_rows, preferred_element_type=jnp.float32).astype(
        jnp.bfloat16
    )
    upper_cells = passed_along(potential, "grp", -1)
    extended = jnp.concatenate([potential[0], upper_cells[0]], axis=0)

    def cut_window(first_row):
        return lax.dynamic_slice_in_dim(extended, first_row, NB, 0)

    window = jax.vmap(cut_window)(slot_offset)
    layered = slot_blips.reshape(slot_count, NB, plane_cells)
    y_value = jnp.einsum("ya,sab->syb", spline, layered, preferred_element_type=jnp.float32).astype(
        jnp.bfloat16
    )
    y_curve = jnp.einsum("ya,sab->syb", second, layered, preferred_element_type=jnp.float32).astype(
        jnp.bfloat16
    )
    flat_value = y_value.reshape(-1, plane_cells)
    values_grid = jnp.dot(flat_value, plane_value, preferred_element_type=jnp.float32)
    laplace = jnp.dot(
        y_curve.reshape(-1, plane_cells), plane_value, preferred_element_type=jnp.float32
    ) + jnp.dot(flat_value, plane_curve, preferred_element_type=jnp.float32)
    applied = (-0.5 * laplace + window.reshape(-1, plane_cells) * values_grid).astype(jnp.bfloat16)
    values_low = values_grid.astype(jnp.bfloat16)
    back_plane = jnp.dot(applied, plane_value, preferred_element_type=jnp.float32).astype(
        jnp.bfloat16
    )
    gradient_piece = jnp.einsum(
        "ay,sab->syb",
        spline,
        back_plane.reshape(slot_count, NB, plane_cells),
        preferred_element_type=jnp.float32,
    ).astype(jnp.bfloat16)
    intersection = lax.dot_general(
        values_low.reshape(slot_count, cell_count),
        applied.reshape(slot_count, cell_count),
        (((1,), (1,)), ((), ())),
        preferred_element_type=jnp.float32,
    ) / float(cell_count)
    select_full = (target[:, None] == jnp.arange(group_size, dtype=jnp.int32)[None, :]).astype(
        jnp.float32
    )
    weighted = jnp.dot(intersection, select_full, precision=lax.Precision.HIGHEST)
    place_f32 = place_hot.astype(jnp.float32)
    send_ham = jnp.concatenate(
        [
            jnp.dot(place_f32, weighted, precision=lax.Precision.HIGHEST),
            asked_rows.astype(jnp.float32)[:, None],
        ],
        axis=1,
    ).reshape(domain_count, capacity, group_size + 1)
    got_ham = lax.all_to_all(send_ham, "dom", split_axis=0, concat_axis=0, tiled=True).reshape(
        domain_count * capacity, group_size + 1
    )
    got_rows = got_ham[:, group_size]
    send_grad = jnp.dot(
        place_low,
        gradient_piece.reshape(slot_count, cell_count),
        preferred_element_type=jnp.bfloat16,
    ).reshape(domain_count, capacity, cell_count)
    got_grad = lax.all_to_all(send_grad, "dom", split_axis=0, concat_axis=0, tiled=True)
    row_hot = got_rows[None, :] == jnp.arange(owned_count, dtype=jnp.float32)[:, None]
    hamilton = jnp.dot(
        row_hot.astype(jnp.float32), got_ham[:, :group_size], precision=lax.Precision.HIGHEST
    )
    gradient = jnp.dot(
        row_hot.astype(jnp.bfloat16),
        got_grad.reshape(-1, cell_count),
        preferred_element_type=jnp.float32,
    )
    return (gradient, hamilton)


def solution(mesh):
    placed = (
        P(("grp", "dom"), None),
        P("dom", "grp", None),
        P(("grp", "dom"), None),
        P(("grp", "dom")),
        P(("grp", "dom")),
    )
    return jax.shard_map(
        on_device,
        mesh=mesh,
        in_specs=placed,
        out_specs=(P(("grp", "dom"), None), P(("grp", "dom"), None)),
        check_vma=False,
    )
```

```python
import jax
import jax.numpy as jnp
from jax import lax
from jax.sharding import PartitionSpec as P

NB = 32


def passed_along(block, axis, distance):
    devices = range(lax.axis_size(axis))
    route = [((i - distance) % len(devices), i) for i in devices]
    return lax.ppermute(block, axis, route)


def spline_tables():
    cells_line = jnp.arange(NB, dtype=jnp.int32)
    offset = cells_line[:, None] - cells_line[None, :]
    spline = jnp.where(
        offset == 0, 2.0 / 3.0, jnp.where(jnp.abs(offset) == 1, 1.0 / 6.0, 0.0)
    ).astype(jnp.float32)
    second = jnp.where(offset == 0, -2.0, jnp.where(jnp.abs(offset) == 1, 1.0, 0.0)).astype(
        jnp.float32
    )
    plane_value = jnp.einsum("ac,bd->abcd", spline, spline).reshape(NB * NB, NB * NB)
    plane_curve = (
        jnp.einsum("ac,bd->abcd", second, spline) + jnp.einsum("ac,bd->abcd", spline, second)
    ).reshape(NB * NB, NB * NB)
    return (
        spline.astype(jnp.bfloat16),
        second.astype(jnp.bfloat16),
        plane_value.astype(jnp.bfloat16),
        plane_curve.astype(jnp.bfloat16),
    )


def on_device(owned_blips, potential, slot_owner, slot_row, slot_offset):
    spline, second, plane_value, plane_curve = spline_tables()
    domain_count = lax.axis_size("dom")
    slot_count = slot_row.shape[0]
    owned_count = owned_blips.shape[0]
    cell_count = owned_blips.shape[1]
    plane_cells = NB * NB
    capacity = max(2, -(-slot_count // domain_count))
    group_size = domain_count * owned_count
    owner_of = slot_owner[:, 0]
    target = owner_of * owned_count + slot_row
    owner_hot = (owner_of[:, None] == jnp.arange(domain_count, dtype=jnp.int32)[None, :]).astype(
        jnp.int32
    )
    position = jnp.sum(jnp.cumsum(owner_hot, axis=0) * owner_hot, axis=1) - 1
    place_slot = owner_of * capacity + position
    place_hot = place_slot[None, :] == jnp.arange(domain_count * capacity, dtype=jnp.int32)[:, None]
    asked_rows = jnp.sum(jnp.where(place_hot, slot_row[None, :], 0), axis=1) + owned_count * (
        1 - jnp.sum(place_hot.astype(jnp.int32), axis=1)
    )
    blocks = owned_blips.reshape(owned_count, NB, plane_cells)
    gathered_blocks = lax.all_gather(blocks, "dom", axis=0, tiled=True)
    slot_blips = jnp.take(gathered_blocks, target, axis=0, mode="clip")
    upper_cells = passed_along(potential, "grp", -1)
    extended = jnp.concatenate([potential[0], upper_cells[0]], axis=0)

    def cut_window(first_row):
        return lax.dynamic_slice_in_dim(extended, first_row, NB, 0)

    window = jax.vmap(cut_window)(slot_offset)
    layered = slot_blips
    y_value = jnp.einsum("ya,sab->syb", spline, layered, preferred_element_type=jnp.float32).astype(
        jnp.bfloat16
    )
    y_curve = jnp.einsum("ya,sab->syb", second, layered, preferred_element_type=jnp.float32).astype(
        jnp.bfloat16
    )
    flat_value = y_value.reshape(-1, plane_cells)
    values_grid = jnp.dot(flat_value, plane_value, preferred_element_type=jnp.float32)
    laplace = jnp.dot(
        y_curve.reshape(-1, plane_cells), plane_value, preferred_element_type=jnp.float32
    ) + jnp.dot(flat_value, plane_curve, preferred_element_type=jnp.float32)
    applied = (-0.5 * laplace + window.reshape(-1, plane_cells) * values_grid).astype(jnp.bfloat16)
    values_low = values_grid.astype(jnp.bfloat16)
    back_plane = jnp.dot(applied, plane_value, preferred_element_type=jnp.float32).astype(
        jnp.bfloat16
    )
    gradient_piece = jnp.einsum(
        "ay,sab->syb",
        spline,
        back_plane.reshape(slot_count, NB, plane_cells),
        preferred_element_type=jnp.float32,
    ).astype(jnp.bfloat16)
    intersection = lax.dot_general(
        values_low.reshape(slot_count, cell_count),
        applied.reshape(slot_count, cell_count),
        (((1,), (1,)), ((), ())),
        preferred_element_type=jnp.float32,
    ) / float(cell_count)
    select_full = (target[:, None] == jnp.arange(group_size, dtype=jnp.int32)[None, :]).astype(
        jnp.float32
    )
    weighted = jnp.dot(intersection, select_full, precision=lax.Precision.HIGHEST)
    place_f32 = place_hot.astype(jnp.float32)
    send_ham = jnp.concatenate(
        [
            jnp.dot(place_f32, weighted, precision=lax.Precision.HIGHEST),
            asked_rows.astype(jnp.float32)[:, None],
        ],
        axis=1,
    ).reshape(domain_count, capacity, group_size + 1)
    got_ham = lax.all_to_all(send_ham, "dom", split_axis=0, concat_axis=0, tiled=True).reshape(
        domain_count * capacity, group_size + 1
    )
    got_rows = got_ham[:, group_size]
    piece_of_place = jnp.sum(
        jnp.where(place_hot, jnp.arange(slot_count, dtype=jnp.int32)[None, :], 0), axis=1
    )
    send_grad = jnp.take(
        gradient_piece.reshape(slot_count, NB, plane_cells), piece_of_place, axis=0, mode="clip"
    ).reshape(domain_count, capacity * NB, plane_cells)
    got_grad = lax.all_to_all(send_grad, "dom", split_axis=0, concat_axis=0, tiled=True).reshape(
        domain_count * capacity, NB, plane_cells
    )
    row_hot = got_rows[None, :] == jnp.arange(owned_count, dtype=jnp.float32)[:, None]
    hamilton = jnp.dot(
        row_hot.astype(jnp.float32), got_ham[:, :group_size], precision=lax.Precision.HIGHEST
    )
    gradient = jnp.einsum(
        "rs,syc->ryc", row_hot.astype(jnp.bfloat16), got_grad, preferred_element_type=jnp.float32
    ).reshape(owned_count, cell_count)
    return (gradient, hamilton)


def solution(mesh):
    placed = (
        P(("grp", "dom"), None),
        P("dom", "grp", None),
        P(("grp", "dom"), None),
        P(("grp", "dom")),
        P(("grp", "dom")),
    )
    return jax.shard_map(
        on_device,
        mesh=mesh,
        in_specs=placed,
        out_specs=(P(("grp", "dom"), None), P(("grp", "dom"), None)),
        check_vma=False,
    )
```

```python
import jax
import jax.numpy as jnp
from jax import lax
from jax.sharding import PartitionSpec as P


NB = 32


def passed_along(block, axis, distance):
    devices = range(lax.axis_size(axis))
    route = [((i - distance) % len(devices), i) for i in devices]
    return lax.ppermute(block, axis, route)


def spline_tables():
    cells_line = jnp.arange(NB, dtype=jnp.int32)
    offset = cells_line[:, None] - cells_line[None, :]
    spline = jnp.where(
        offset == 0, 2.0 / 3.0, jnp.where(jnp.abs(offset) == 1, 1.0 / 6.0, 0.0)
    ).astype(jnp.float32)
    second = jnp.where(offset == 0, -2.0, jnp.where(jnp.abs(offset) == 1, 1.0, 0.0)).astype(
        jnp.float32
    )
    plane_value = jnp.einsum("ac,bd->abcd", spline, spline).reshape(NB * NB, NB * NB)
    plane_curve = (
        jnp.einsum("ac,bd->abcd", second, spline) + jnp.einsum("ac,bd->abcd", spline, second)
    ).reshape(NB * NB, NB * NB)
    return (
        spline.astype(jnp.bfloat16),
        second.astype(jnp.bfloat16),
        plane_value.astype(jnp.bfloat16),
        plane_curve.astype(jnp.bfloat16),
    )


def on_device(owned_blips, potential, slot_owner, slot_row, slot_offset):
    spline, second, plane_value, plane_curve = spline_tables()
    domain_count = lax.axis_size("dom")
    slot_count = slot_row.shape[0]
    owned_count = owned_blips.shape[0]
    cell_count = owned_blips.shape[1]
    plane_cells = NB * NB
    capacity = max(2, -(-slot_count // domain_count))
    group_size = domain_count * owned_count
    owner_of = slot_owner[:, 0]
    target = owner_of * owned_count + slot_row
    owner_hot = (owner_of[:, None] == jnp.arange(domain_count, dtype=jnp.int32)[None, :]).astype(
        jnp.int32
    )
    position = jnp.sum(jnp.cumsum(owner_hot, axis=0) * owner_hot, axis=1) - 1
    place_slot = owner_of * capacity + position
    place_hot = place_slot[None, :] == jnp.arange(domain_count * capacity, dtype=jnp.int32)[:, None]
    asked_rows = jnp.sum(jnp.where(place_hot, slot_row[None, :], 0), axis=1) + owned_count * (
        1 - jnp.sum(place_hot.astype(jnp.int32), axis=1)
    )
    blocks = owned_blips.reshape(owned_count, NB, plane_cells)
    half = plane_cells // 2
    early = half - 4 * NB
    gathered_a = lax.all_gather(blocks[:, :, :half], "dom", axis=0, tiled=True)
    gathered_b = lax.all_gather(blocks[:, :, half:], "dom", axis=0, tiled=True)
    blips_a = jnp.take(gathered_a, target, axis=0, mode="clip")
    blips_b = jnp.take(gathered_b, target, axis=0, mode="clip")
    upper_cells = passed_along(potential, "grp", -1)
    extended = jnp.concatenate([potential[0], upper_cells[0]], axis=0)

    def cut_window(first_row):
        return lax.dynamic_slice_in_dim(extended, first_row, NB, 0)

    window = jax.vmap(cut_window)(slot_offset)

    def y_pass(table, layered):
        return jnp.einsum(
            "ya,sab->syb", table, layered, preferred_element_type=jnp.float32
        ).astype(jnp.bfloat16)

    def flat(block):
        return block.reshape(-1, block.shape[-1])

    def plane_terms(y_value, y_curve, value_cols, curve_cols, window_cols):
        values_grid = jnp.dot(flat(y_value), value_cols, preferred_element_type=jnp.float32)
        laplace = jnp.dot(flat(y_curve), value_cols, preferred_element_type=jnp.float32) + jnp.dot(
            flat(y_value), curve_cols, preferred_element_type=jnp.float32
        )
        applied = (-0.5 * laplace + flat(window_cols) * values_grid).astype(jnp.bfloat16)
        return applied, values_grid.astype(jnp.bfloat16)

    def gradient_of(applied_rows, value_cols):
        back_plane = jnp.dot(applied_rows, value_cols, preferred_element_type=jnp.float32).astype(
            jnp.bfloat16
        )
        return jnp.einsum(
            "ay,sab->syb",
            spline,
            back_plane.reshape(slot_count, NB, -1),
            preferred_element_type=jnp.float32,
        ).astype(jnp.bfloat16)

    piece_of_place = jnp.sum(
        jnp.where(place_hot, jnp.arange(slot_count, dtype=jnp.int32)[None, :], 0), axis=1
    )

    def send_gradient(gradient_piece):
        send = jnp.take(gradient_piece, piece_of_place, axis=0, mode="clip")
        send = send.reshape(domain_count, capacity * NB, send.shape[-1])
        got = lax.all_to_all(send, "dom", split_axis=0, concat_axis=0, tiled=True)
        return got.reshape(domain_count * capacity, NB, -1)

    y_value_a = y_pass(spline, blips_a)
    y_curve_a = y_pass(second, blips_a)
    applied_a, values_low_a = plane_terms(
        y_value_a,
        y_curve_a,
        plane_value[:half, :half],
        plane_curve[:half, :half],
        window[:, :, :half],
    )
    gradient_a = gradient_of(applied_a, plane_value[:half, :early])
    got_grad_a = send_gradient(gradient_a)
    y_value = jnp.concatenate([y_value_a, y_pass(spline, blips_b)], axis=2)
    y_curve = jnp.concatenate([y_curve_a, y_pass(second, blips_b)], axis=2)
    applied_b, values_low_b = plane_terms(
        y_value, y_curve, plane_value[:, early:], plane_curve[:, early:], window[:, :, early:]
    )
    applied_rows = jnp.concatenate([applied_a[:, :early], applied_b], axis=1)
    gradient_b = gradient_of(applied_rows, plane_value[:, early:])
    got_grad_b = send_gradient(gradient_b)


    def overlap(values_low, applied):
        return lax.dot_general(
            values_low.reshape(slot_count, NB, -1),
            applied.reshape(slot_count, NB, -1),
            (((1, 2), (1, 2)), ((), ())),
            preferred_element_type=jnp.float32,
        )

    intersection = (
        overlap(values_low_a[:, :early], applied_a[:, :early]) + overlap(values_low_b, applied_b)
    ) / float(cell_count)
    select_full = (target[:, None] == jnp.arange(group_size, dtype=jnp.int32)[None, :]).astype(
        jnp.float32
    )
    weighted = jnp.dot(intersection, select_full, precision=lax.Precision.HIGHEST)
    place_f32 = place_hot.astype(jnp.float32)
    send_ham = jnp.concatenate(
        [
            jnp.dot(place_f32, weighted, precision=lax.Precision.HIGHEST),
            asked_rows.astype(jnp.float32)[:, None],
        ],
        axis=1,
    ).reshape(domain_count, capacity, group_size + 1)
    shared_ham = lax.all_gather(send_ham, "dom", axis=0, tiled=True).reshape(
        domain_count, domain_count, capacity, group_size + 1
    )
    got_ham = lax.dynamic_slice_in_dim(shared_ham, lax.axis_index("dom"), 1, axis=1).reshape(
        domain_count * capacity, group_size + 1
    )
    got_rows = got_ham[:, group_size]
    row_hot = got_rows[None, :] == jnp.arange(owned_count, dtype=jnp.float32)[:, None]
    hamilton = jnp.dot(
        row_hot.astype(jnp.float32), got_ham[:, :group_size], precision=lax.Precision.HIGHEST
    )
    row_low = row_hot.astype(jnp.bfloat16)
    gradient = jnp.concatenate(
        [
            jnp.einsum("rs,syc->ryc", row_low, got, preferred_element_type=jnp.float32)
            for got in (got_grad_a, got_grad_b)
        ],
        axis=2,
    ).reshape(owned_count, cell_count)
    return (gradient, hamilton)


def solution(mesh):
    placed = (
        P(("grp", "dom"), None),
        P("dom", "grp", None),
        P(("grp", "dom"), None),
        P(("grp", "dom")),
        P(("grp", "dom")),
    )
    return jax.shard_map(
        on_device,
        mesh=mesh,
        in_specs=placed,
        out_specs=(P(("grp", "dom"), None), P(("grp", "dom"), None)),
        check_vma=False,
    )
```

```python
import jax
import jax.numpy as jnp
from jax import lax
from jax.sharding import PartitionSpec as P


NB = 32


def passed_along(block, axis, distance):
    devices = range(lax.axis_size(axis))
    route = [((i - distance) % len(devices), i) for i in devices]
    return lax.ppermute(block, axis, route)


def spline_tables():
    cells_line = jnp.arange(NB, dtype=jnp.int32)
    offset = cells_line[:, None] - cells_line[None, :]
    spline = jnp.where(
        offset == 0, 2.0 / 3.0, jnp.where(jnp.abs(offset) == 1, 1.0 / 6.0, 0.0)
    ).astype(jnp.float32)
    second = jnp.where(offset == 0, -2.0, jnp.where(jnp.abs(offset) == 1, 1.0, 0.0)).astype(
        jnp.float32
    )
    plane_value = jnp.einsum("ac,bd->abcd", spline, spline).reshape(NB * NB, NB * NB)
    plane_curve = (
        jnp.einsum("ac,bd->abcd", second, spline) + jnp.einsum("ac,bd->abcd", spline, second)
    ).reshape(NB * NB, NB * NB)
    return (
        spline.astype(jnp.bfloat16),
        second.astype(jnp.bfloat16),
        plane_value.astype(jnp.bfloat16),
        plane_curve.astype(jnp.bfloat16),
    )


def on_device(owned_blips, potential, slot_owner, slot_row, slot_offset):
    spline, second, plane_value, plane_curve = spline_tables()
    domain_count = lax.axis_size("dom")
    slot_count = slot_row.shape[0]
    owned_count = owned_blips.shape[0]
    cell_count = owned_blips.shape[1]
    plane_cells = NB * NB
    capacity = max(2, -(-slot_count // domain_count))
    group_size = domain_count * owned_count
    owner_of = slot_owner[:, 0]
    target = owner_of * owned_count + slot_row
    owner_hot = (owner_of[:, None] == jnp.arange(domain_count, dtype=jnp.int32)[None, :]).astype(
        jnp.int32
    )
    position = jnp.sum(jnp.cumsum(owner_hot, axis=0) * owner_hot, axis=1) - 1
    place_slot = owner_of * capacity + position
    place_hot = place_slot[None, :] == jnp.arange(domain_count * capacity, dtype=jnp.int32)[:, None]
    asked_rows = jnp.sum(jnp.where(place_hot, slot_row[None, :], 0), axis=1) + owned_count * (
        1 - jnp.sum(place_hot.astype(jnp.int32), axis=1)
    )
    blocks = owned_blips.reshape(owned_count, NB, plane_cells)
    half = plane_cells // 2
    early = half - 4 * NB
    asked_of_me = lax.all_to_all(
        asked_rows.reshape(domain_count, capacity), "dom", split_axis=0, concat_axis=0, tiled=True
    ).reshape(-1)
    lent = jnp.take(blocks[:, :, :half], asked_of_me, axis=0, mode="clip")
    fetched_a = lax.all_to_all(
        lent.reshape(domain_count, capacity * NB, half),
        "dom",
        split_axis=0,
        concat_axis=0,
        tiled=True,
    ).reshape(domain_count * capacity, NB, half)
    gathered_b = lax.all_gather(blocks[:, :, half:], "dom", axis=0, tiled=True)
    blips_a = jnp.take(fetched_a, place_slot, axis=0, mode="clip")
    blips_b = jnp.take(gathered_b, target, axis=0, mode="clip")
    upper_cells = passed_along(potential, "grp", -1)
    extended = jnp.concatenate([potential[0], upper_cells[0]], axis=0)

    def cut_window(first_row):
        return lax.dynamic_slice_in_dim(extended, first_row, NB, 0)

    window = jax.vmap(cut_window)(slot_offset)

    def y_pass(table, layered):
        return jnp.einsum(
            "ya,sab->syb", table, layered, preferred_element_type=jnp.float32
        ).astype(jnp.bfloat16)

    def flat(block):
        return block.reshape(-1, block.shape[-1])

    def plane_terms(y_value, y_curve, value_cols, curve_cols, window_cols):
        values_grid = jnp.dot(flat(y_value), value_cols, preferred_element_type=jnp.float32)
        laplace = jnp.dot(flat(y_curve), value_cols, preferred_element_type=jnp.float32) + jnp.dot(
            flat(y_value), curve_cols, preferred_element_type=jnp.float32
        )
        applied = (-0.5 * laplace + flat(window_cols) * values_grid).astype(jnp.bfloat16)
        return applied, values_grid.astype(jnp.bfloat16)

    def gradient_of(applied_rows, value_cols):
        back_plane = jnp.dot(applied_rows, value_cols, preferred_element_type=jnp.float32).astype(
            jnp.bfloat16
        )
        return jnp.einsum(
            "ay,sab->syb",
            spline,
            back_plane.reshape(slot_count, NB, -1),
            preferred_element_type=jnp.float32,
        ).astype(jnp.bfloat16)

    piece_of_place = jnp.sum(
        jnp.where(place_hot, jnp.arange(slot_count, dtype=jnp.int32)[None, :], 0), axis=1
    )

    def send_gradient(gradient_piece):
        send = jnp.take(gradient_piece, piece_of_place, axis=0, mode="clip")
        send = send.reshape(domain_count, capacity * NB, send.shape[-1])
        got = lax.all_to_all(send, "dom", split_axis=0, concat_axis=0, tiled=True)
        return got.reshape(domain_count * capacity, NB, -1)

    y_value_a = y_pass(spline, blips_a)
    y_curve_a = y_pass(second, blips_a)
    applied_a, values_low_a = plane_terms(
        y_value_a,
        y_curve_a,
        plane_value[:half, :half],
        plane_curve[:half, :half],
        window[:, :, :half],
    )
    gradient_a = gradient_of(applied_a, plane_value[:half, :early])
    got_grad_a = send_gradient(gradient_a)
    y_value = jnp.concatenate([y_value_a, y_pass(spline, blips_b)], axis=2)
    y_curve = jnp.concatenate([y_curve_a, y_pass(second, blips_b)], axis=2)
    applied_b, values_low_b = plane_terms(
        y_value, y_curve, plane_value[:, early:], plane_curve[:, early:], window[:, :, early:]
    )
    applied_rows = jnp.concatenate([applied_a[:, :early], applied_b], axis=1)
    gradient_b = gradient_of(applied_rows, plane_value[:, early:])
    got_grad_b = send_gradient(gradient_b)


    def overlap(values_low, applied):
        return lax.dot_general(
            values_low.reshape(slot_count, NB, -1),
            applied.reshape(slot_count, NB, -1),
            (((1, 2), (1, 2)), ((), ())),
            preferred_element_type=jnp.float32,
        )

    intersection = (
        overlap(values_low_a[:, :early], applied_a[:, :early]) + overlap(values_low_b, applied_b)
    ) / float(cell_count)
    select_full = (target[:, None] == jnp.arange(group_size, dtype=jnp.int32)[None, :]).astype(
        jnp.float32
    )
    weighted = jnp.dot(intersection, select_full, precision=lax.Precision.HIGHEST)
    send_ham = jnp.dot(
        place_hot.astype(jnp.float32), weighted, precision=lax.Precision.HIGHEST
    ).reshape(domain_count, capacity, group_size)
    got_ham = lax.all_to_all(send_ham, "dom", split_axis=0, concat_axis=0, tiled=True).reshape(
        domain_count * capacity, group_size
    )
    row_hot = asked_of_me[None, :] == jnp.arange(owned_count, dtype=jnp.int32)[:, None]
    hamilton = jnp.dot(row_hot.astype(jnp.float32), got_ham, precision=lax.Precision.HIGHEST)
    row_low = row_hot.astype(jnp.bfloat16)
    gradient = jnp.concatenate(
        [
            jnp.einsum("rs,syc->ryc", row_low, got, preferred_element_type=jnp.float32)
            for got in (got_grad_a, got_grad_b)
        ],
        axis=2,
    ).reshape(owned_count, cell_count)
    return (gradient, hamilton)


def solution(mesh):
    placed = (
        P(("grp", "dom"), None),
        P("dom", "grp", None),
        P(("grp", "dom"), None),
        P(("grp", "dom")),
        P(("grp", "dom")),
    )
    return jax.shard_map(
        on_device,
        mesh=mesh,
        in_specs=placed,
        out_specs=(P(("grp", "dom"), None), P(("grp", "dom"), None)),
        check_vma=False,
    )
```

```python
import jax
import jax.numpy as jnp
from jax import lax
from jax.sharding import PartitionSpec as P


NB = 32


def passed_along(block, axis, distance):
    devices = range(lax.axis_size(axis))
    route = [((i - distance) % len(devices), i) for i in devices]
    return lax.ppermute(block, axis, route)


def line_tables(offset):
    spline = jnp.where(offset == 0, 2.0 / 3.0, jnp.where(jnp.abs(offset) == 1, 1.0 / 6.0, 0.0))
    second = jnp.where(offset == 0, -2.0, jnp.where(jnp.abs(offset) == 1, 1.0, 0.0))
    return spline.astype(jnp.float32), second.astype(jnp.float32)


def spline_tables():
    cells_line = jnp.arange(NB, dtype=jnp.int32)
    spline, second = line_tables(cells_line[:, None] - cells_line[None, :])
    rows = lax.broadcasted_iota(jnp.int32, (NB * NB, NB * NB), 0)
    cols = lax.broadcasted_iota(jnp.int32, (NB * NB, NB * NB), 1)
    spline_x, second_x = line_tables(rows // NB - cols // NB)
    spline_z, second_z = line_tables(rows % NB - cols % NB)
    plane_value = spline_x * spline_z
    plane_curve = second_x * spline_z + spline_x * second_z
    return (
        spline.astype(jnp.bfloat16),
        second.astype(jnp.bfloat16),
        plane_value.astype(jnp.bfloat16),
        plane_curve.astype(jnp.bfloat16),
    )


def on_device(owned_blips, potential, slot_owner, slot_row, slot_offset):
    spline, second, plane_value, plane_curve = spline_tables()
    domain_count = lax.axis_size("dom")
    slot_count = slot_row.shape[0]
    owned_count = owned_blips.shape[0]
    cell_count = owned_blips.shape[1]
    plane_cells = NB * NB
    capacity = max(2, -(-slot_count // domain_count))
    group_size = domain_count * owned_count
    owner_of = slot_owner[:, 0]
    target = owner_of * owned_count + slot_row
    owner_hot = (owner_of[:, None] == jnp.arange(domain_count, dtype=jnp.int32)[None, :]).astype(
        jnp.int32
    )
    position = jnp.sum(jnp.cumsum(owner_hot, axis=0) * owner_hot, axis=1) - 1
    place_slot = owner_of * capacity + position
    place_hot = place_slot[None, :] == jnp.arange(domain_count * capacity, dtype=jnp.int32)[:, None]
    asked_rows = jnp.sum(jnp.where(place_hot, slot_row[None, :], 0), axis=1) + owned_count * (
        1 - jnp.sum(place_hot.astype(jnp.int32), axis=1)
    )
    blocks = owned_blips.reshape(owned_count, NB, plane_cells)
    half = 3 * plane_cells // 8
    early = plane_cells // 4
    asked_of_me = lax.all_to_all(
        asked_rows.reshape(domain_count, capacity), "dom", split_axis=0, concat_axis=0, tiled=True
    ).reshape(-1)
    lent = jnp.take(blocks[:, :, :half], asked_of_me, axis=0, mode="clip")
    fetched_a = lax.all_to_all(
        lent.reshape(domain_count, capacity * NB, half),
        "dom",
        split_axis=0,
        concat_axis=0,
        tiled=True,
    ).reshape(domain_count * capacity, NB, half)
    gathered_b = lax.all_gather(blocks[:, :, half:], "dom", axis=0, tiled=True)
    blips_a = jnp.take(fetched_a, place_slot, axis=0, mode="clip")
    blips_b = jnp.take(gathered_b, target, axis=0, mode="clip")
    upper_cells = passed_along(potential, "grp", -1)
    extended = jnp.concatenate([potential[0], upper_cells[0]], axis=0)

    window = jnp.take(
        extended, slot_offset[:, None] + jnp.arange(NB, dtype=jnp.int32)[None, :], axis=0, mode="clip"
    )

    def y_pass(table, layered):
        return jnp.einsum(
            "ya,sab->syb", table, layered, preferred_element_type=jnp.float32
        ).astype(jnp.bfloat16)

    def flat(block):
        return block.reshape(-1, block.shape[-1])

    def plane_terms(y_value, y_curve, value_cols, curve_cols, window_cols):
        values_grid = jnp.dot(flat(y_value), value_cols, preferred_element_type=jnp.float32)
        laplace = jnp.dot(flat(y_curve), value_cols, preferred_element_type=jnp.float32) + jnp.dot(
            flat(y_value), curve_cols, preferred_element_type=jnp.float32
        )
        applied = (-0.5 * laplace + flat(window_cols) * values_grid).astype(jnp.bfloat16)
        return applied, values_grid.astype(jnp.bfloat16)

    def gradient_of(applied_rows, value_cols):
        back_plane = jnp.dot(applied_rows, value_cols, preferred_element_type=jnp.float32).astype(
            jnp.bfloat16
        )
        return jnp.einsum(
            "ay,sab->syb",
            spline,
            back_plane.reshape(slot_count, NB, -1),
            preferred_element_type=jnp.float32,
        ).astype(jnp.bfloat16)

    piece_of_place = jnp.sum(
        jnp.where(place_hot, jnp.arange(slot_count, dtype=jnp.int32)[None, :], 0), axis=1
    )

    def send_gradient(gradient_piece):
        send = jnp.take(gradient_piece, piece_of_place, axis=0, mode="clip")
        send = send.reshape(domain_count, capacity * NB, send.shape[-1])
        got = lax.all_to_all(send, "dom", split_axis=0, concat_axis=0, tiled=True)
        return got.reshape(domain_count * capacity, NB, -1)

    y_value_a = y_pass(spline, blips_a)
    y_curve_a = y_pass(second, blips_a)
    applied_a, values_low_a = plane_terms(
        y_value_a,
        y_curve_a,
        plane_value[:half, :half],
        plane_curve[:half, :half],
        window[:, :, :half],
    )
    gradient_a = gradient_of(applied_a, plane_value[:half, :early])
    got_grad_a = send_gradient(gradient_a)
    y_value = jnp.concatenate([y_value_a, y_pass(spline, blips_b)], axis=2)
    y_curve = jnp.concatenate([y_curve_a, y_pass(second, blips_b)], axis=2)
    applied_b, values_low_b = plane_terms(
        y_value, y_curve, plane_value[:, early:], plane_curve[:, early:], window[:, :, early:]
    )
    applied_rows = jnp.concatenate([applied_a[:, :early], applied_b], axis=1)
    gradient_b = gradient_of(applied_rows, plane_value[:, early:])
    got_grad_b = send_gradient(gradient_b)


    def overlap(values_low, applied):
        return lax.dot_general(
            values_low.reshape(slot_count, NB, -1),
            applied.reshape(slot_count, NB, -1),
            (((1, 2), (1, 2)), ((), ())),
            preferred_element_type=jnp.float32,
        )

    intersection = (
        overlap(values_low_a[:, :early], applied_a[:, :early]) + overlap(values_low_b, applied_b)
    ) / float(cell_count)
    select_full = (target[:, None] == jnp.arange(group_size, dtype=jnp.int32)[None, :]).astype(
        jnp.float32
    )
    weighted = jnp.dot(intersection, select_full, precision=lax.Precision.HIGHEST)
    send_ham = jnp.dot(
        place_hot.astype(jnp.float32), weighted, precision=lax.Precision.HIGHEST
    ).reshape(domain_count, capacity, group_size)
    got_ham = lax.all_to_all(send_ham, "dom", split_axis=0, concat_axis=0, tiled=True).reshape(
        domain_count * capacity, group_size
    )
    row_hot = asked_of_me[None, :] == jnp.arange(owned_count, dtype=jnp.int32)[:, None]
    hamilton = jnp.dot(row_hot.astype(jnp.float32), got_ham, precision=lax.Precision.HIGHEST)
    row_low = row_hot.astype(jnp.bfloat16)
    gradient = jnp.concatenate(
        [
            jnp.einsum("rs,syc->ryc", row_low, got, preferred_element_type=jnp.float32)
            for got in (got_grad_a, got_grad_b)
        ],
        axis=2,
    ).reshape(owned_count, cell_count)
    return (gradient, hamilton)


def solution(mesh):
    placed = (
        P(("grp", "dom"), None),
        P("dom", "grp", None),
        P(("grp", "dom"), None),
        P(("grp", "dom")),
        P(("grp", "dom")),
    )
    return jax.shard_map(
        on_device,
        mesh=mesh,
        in_specs=placed,
        out_specs=(P(("grp", "dom"), None), P(("grp", "dom"), None)),
        check_vma=False,
    )
```

```python
import jax
import jax.numpy as jnp
from jax import lax
from jax.sharding import PartitionSpec as P


NB = 32


def passed_along(block, axis, distance):
    devices = range(lax.axis_size(axis))
    route = [((i - distance) % len(devices), i) for i in devices]
    return lax.ppermute(block, axis, route)


def line_tables(offset):
    spline = jnp.where(offset == 0, 2.0 / 3.0, jnp.where(jnp.abs(offset) == 1, 1.0 / 6.0, 0.0))
    second = jnp.where(offset == 0, -2.0, jnp.where(jnp.abs(offset) == 1, 1.0, 0.0))
    return spline.astype(jnp.float32), second.astype(jnp.float32)


def spline_tables():
    cells_line = jnp.arange(NB, dtype=jnp.int32)
    spline, second = line_tables(cells_line[:, None] - cells_line[None, :])
    rows = lax.broadcasted_iota(jnp.int32, (NB * NB, NB * NB), 0)
    cols = lax.broadcasted_iota(jnp.int32, (NB * NB, NB * NB), 1)
    spline_x, second_x = line_tables(rows // NB - cols // NB)
    spline_z, second_z = line_tables(rows % NB - cols % NB)
    plane_value = spline_x * spline_z
    plane_curve = second_x * spline_z + spline_x * second_z
    return (
        spline.astype(jnp.bfloat16),
        second.astype(jnp.bfloat16),
        plane_value.astype(jnp.bfloat16),
        plane_curve.astype(jnp.bfloat16),
    )


def on_device(owned_blips, potential, slot_owner, slot_row, slot_offset):
    spline, second, plane_value, plane_curve = spline_tables()
    domain_count = lax.axis_size("dom")
    slot_count = slot_row.shape[0]
    owned_count = owned_blips.shape[0]
    cell_count = owned_blips.shape[1]
    plane_cells = NB * NB
    capacity = max(2, -(-slot_count // domain_count))
    group_size = domain_count * owned_count
    owner_of = slot_owner[:, 0]
    target = owner_of * owned_count + slot_row
    owner_hot = (owner_of[:, None] == jnp.arange(domain_count, dtype=jnp.int32)[None, :]).astype(
        jnp.int32
    )
    position = jnp.sum(jnp.cumsum(owner_hot, axis=0) * owner_hot, axis=1) - 1
    place_slot = owner_of * capacity + position
    place_hot = place_slot[None, :] == jnp.arange(domain_count * capacity, dtype=jnp.int32)[:, None]
    asked_rows = jnp.sum(jnp.where(place_hot, slot_row[None, :], 0), axis=1) + owned_count * (
        1 - jnp.sum(place_hot.astype(jnp.int32), axis=1)
    )
    blocks = owned_blips.reshape(owned_count, NB, plane_cells)
    half = 3 * plane_cells // 8
    early = plane_cells // 4
    asked_of_me = lax.all_to_all(
        asked_rows.reshape(domain_count, capacity), "dom", split_axis=0, concat_axis=0, tiled=True
    ).reshape(-1)
    lent = jnp.take(blocks[:, :, :half], asked_of_me, axis=0, mode="clip")
    fetched_a = lax.all_to_all(
        lent.reshape(domain_count, capacity * NB, half),
        "dom",
        split_axis=0,
        concat_axis=0,
        tiled=True,
    ).reshape(domain_count * capacity, NB, half)
    gathered_b = lax.all_gather(blocks[:, :, half:], "dom", axis=0, tiled=True)
    blips_a = jnp.take(fetched_a, place_slot, axis=0, mode="clip")
    blips_b = jnp.take(gathered_b, target, axis=0, mode="clip")
    upper_cells = passed_along(potential, "grp", -1)
    extended = jnp.concatenate([potential[0], upper_cells[0]], axis=0)

    window = jnp.take(
        extended, slot_offset[:, None] + jnp.arange(NB, dtype=jnp.int32)[None, :], axis=0, mode="clip"
    )

    def y_pass(table, layered):
        return jnp.einsum(
            "ya,sab->syb", table, layered, preferred_element_type=jnp.float32
        ).astype(jnp.bfloat16)

    def flat(block):
        return block.reshape(-1, block.shape[-1])

    def plane_terms(y_value, y_curve, value_cols, curve_cols, window_cols):
        values_grid = jnp.dot(flat(y_value), value_cols, preferred_element_type=jnp.float32)
        laplace = jnp.dot(flat(y_curve), value_cols, preferred_element_type=jnp.float32) + jnp.dot(
            flat(y_value), curve_cols, preferred_element_type=jnp.float32
        )
        applied = (-0.5 * laplace + flat(window_cols) * values_grid).astype(jnp.bfloat16)
        return applied, values_grid.astype(jnp.bfloat16)

    def gradient_of(applied_rows, value_cols):
        back_plane = jnp.dot(applied_rows, value_cols, preferred_element_type=jnp.float32).astype(
            jnp.bfloat16
        )
        return jnp.einsum(
            "ay,sab->syb",
            spline,
            back_plane.reshape(slot_count, NB, -1),
            preferred_element_type=jnp.float32,
        ).astype(jnp.bfloat16)

    piece_of_place = jnp.sum(
        jnp.where(place_hot, jnp.arange(slot_count, dtype=jnp.int32)[None, :], 0), axis=1
    )

    def send_gradient(gradient_piece):
        send = jnp.take(gradient_piece, piece_of_place, axis=0, mode="clip")
        send = send.reshape(domain_count, capacity * NB, send.shape[-1])
        got = lax.all_to_all(send, "dom", split_axis=0, concat_axis=0, tiled=True)
        return got.reshape(domain_count * capacity, NB, -1)

    y_value_a = y_pass(spline, blips_a)
    y_curve_a = y_pass(second, blips_a)
    applied_a, values_low_a = plane_terms(
        y_value_a,
        y_curve_a,
        plane_value[:half, :half],
        plane_curve[:half, :half],
        window[:, :, :half],
    )
    gradient_a = gradient_of(applied_a, plane_value[:half, :early])
    got_grad_a = send_gradient(gradient_a)
    y_value = jnp.concatenate([y_value_a, y_pass(spline, blips_b)], axis=2)
    y_curve = jnp.concatenate([y_curve_a, y_pass(second, blips_b)], axis=2)
    applied_b, values_low_b = plane_terms(
        y_value, y_curve, plane_value[:, early:], plane_curve[:, early:], window[:, :, early:]
    )
    applied_rows = jnp.concatenate([applied_a[:, :early], applied_b], axis=1)
    gradient_b = gradient_of(applied_rows, plane_value[:, early:])
    got_grad_b = send_gradient(gradient_b)


    def overlap(values_low, applied):
        return lax.dot_general(
            values_low.reshape(slot_count, NB, -1),
            applied.reshape(slot_count, NB, -1),
            (((1, 2), (1, 2)), ((), ())),
            preferred_element_type=jnp.float32,
        )

    intersection = (
        overlap(values_low_a[:, :early], applied_a[:, :early]) + overlap(values_low_b, applied_b)
    ) / float(cell_count)
    select_full = (target[:, None] == jnp.arange(group_size, dtype=jnp.int32)[None, :]).astype(
        jnp.float32
    )
    weighted = jnp.dot(intersection, select_full, precision=lax.Precision.HIGHEST)
    send_ham = jnp.dot(
        place_hot.astype(jnp.float32), weighted, precision=lax.Precision.HIGHEST
    ).reshape(domain_count, capacity, group_size)
    shared_ham = lax.all_gather(send_ham, "dom", axis=0, tiled=True).reshape(
        domain_count, domain_count, capacity, group_size
    )
    got_ham = lax.dynamic_slice_in_dim(shared_ham, lax.axis_index("dom"), 1, axis=1).reshape(
        domain_count * capacity, group_size
    )
    row_hot = asked_of_me[None, :] == jnp.arange(owned_count, dtype=jnp.int32)[:, None]
    hamilton = jnp.dot(row_hot.astype(jnp.float32), got_ham, precision=lax.Precision.HIGHEST)
    row_low = row_hot.astype(jnp.bfloat16)
    gradient = jnp.concatenate(
        [
            jnp.einsum("rs,syc->ryc", row_low, got, preferred_element_type=jnp.float32)
            for got in (got_grad_a, got_grad_b)
        ],
        axis=2,
    ).reshape(owned_count, cell_count)
    return (gradient, hamilton)


def solution(mesh):
    placed = (
        P(("grp", "dom"), None),
        P("dom", "grp", None),
        P(("grp", "dom"), None),
        P(("grp", "dom")),
        P(("grp", "dom")),
    )
    return jax.shard_map(
        on_device,
        mesh=mesh,
        in_specs=placed,
        out_specs=(P(("grp", "dom"), None), P(("grp", "dom"), None)),
        check_vma=False,
    )
```

```python
import jax
import jax.numpy as jnp
from jax import lax
from jax.sharding import PartitionSpec as P


NB = 32


def passed_along(block, axis, distance):
    devices = range(lax.axis_size(axis))
    route = [((i - distance) % len(devices), i) for i in devices]
    return lax.ppermute(block, axis, route)


def line_tables(offset):
    spline = jnp.where(offset == 0, 2.0 / 3.0, jnp.where(jnp.abs(offset) == 1, 1.0 / 6.0, 0.0))
    second = jnp.where(offset == 0, -2.0, jnp.where(jnp.abs(offset) == 1, 1.0, 0.0))
    return spline.astype(jnp.float32), second.astype(jnp.float32)


def spline_tables():
    cells_line = jnp.arange(NB, dtype=jnp.int32)
    spline, second = line_tables(cells_line[:, None] - cells_line[None, :])
    rows = lax.broadcasted_iota(jnp.int32, (NB * NB, NB * NB), 0)
    cols = lax.broadcasted_iota(jnp.int32, (NB * NB, NB * NB), 1)
    spline_x, second_x = line_tables(rows // NB - cols // NB)
    spline_z, second_z = line_tables(rows % NB - cols % NB)
    plane_value = spline_x * spline_z
    plane_curve = second_x * spline_z + spline_x * second_z
    return (
        spline.astype(jnp.bfloat16),
        second.astype(jnp.bfloat16),
        plane_value.astype(jnp.bfloat16),
        plane_curve.astype(jnp.bfloat16),
    )


def on_device(owned_blips, potential, slot_owner, slot_row, slot_offset):
    spline, second, plane_value, plane_curve = spline_tables()
    domain_count = lax.axis_size("dom")
    slot_count = slot_row.shape[0]
    owned_count = owned_blips.shape[0]
    cell_count = owned_blips.shape[1]
    plane_cells = NB * NB
    capacity = max(2, -(-slot_count // domain_count))
    group_size = domain_count * owned_count
    owner_of = slot_owner[:, 0]
    target = owner_of * owned_count + slot_row
    owner_hot = (owner_of[:, None] == jnp.arange(domain_count, dtype=jnp.int32)[None, :]).astype(
        jnp.int32
    )
    position = jnp.sum(jnp.cumsum(owner_hot, axis=0) * owner_hot, axis=1) - 1
    place_slot = owner_of * capacity + position
    place_hot = place_slot[None, :] == jnp.arange(domain_count * capacity, dtype=jnp.int32)[:, None]
    asked_rows = jnp.sum(jnp.where(place_hot, slot_row[None, :], 0), axis=1) + owned_count * (
        1 - jnp.sum(place_hot.astype(jnp.int32), axis=1)
    )
    blocks = owned_blips.reshape(owned_count, NB, plane_cells)
    half = 3 * plane_cells // 8
    early = plane_cells // 4
    asked_of_me = lax.all_to_all(
        asked_rows.reshape(domain_count, capacity), "dom", split_axis=0, concat_axis=0, tiled=True
    ).reshape(-1)
    lent = jnp.take(blocks[:, :, :half], asked_of_me, axis=0, mode="clip")
    fetched_a = lax.all_to_all(
        lent.reshape(domain_count, capacity * NB, half),
        "dom",
        split_axis=0,
        concat_axis=0,
        tiled=True,
    ).reshape(domain_count * capacity, NB, half)
    gathered_b = lax.all_gather(blocks[:, :, half:], "dom", axis=0, tiled=True)
    blips_a = jnp.take(fetched_a, place_slot, axis=0, mode="clip")
    blips_b = jnp.take(gathered_b, target, axis=0, mode="clip")
    upper_cells = passed_along(potential, "grp", -1)
    extended = jnp.concatenate([potential[0], upper_cells[0]], axis=0)

    window = jnp.take(
        extended, slot_offset[:, None] + jnp.arange(NB, dtype=jnp.int32)[None, :], axis=0, mode="clip"
    )

    def y_pass(table, layered):
        return jnp.einsum(
            "ya,sab->syb", table, layered, preferred_element_type=jnp.float32
        ).astype(jnp.bfloat16)

    def flat(block):
        return block.reshape(-1, block.shape[-1])

    def plane_terms(y_value, y_curve, value_cols, curve_cols, window_cols):
        values_grid = jnp.dot(flat(y_value), value_cols, preferred_element_type=jnp.float32)
        laplace = jnp.dot(flat(y_curve), value_cols, preferred_element_type=jnp.float32) + jnp.dot(
            flat(y_value), curve_cols, preferred_element_type=jnp.float32
        )
        applied = (-0.5 * laplace + flat(window_cols) * values_grid).astype(jnp.bfloat16)
        return applied, values_grid.astype(jnp.bfloat16)

    def gradient_of(applied_rows, value_cols):
        back_plane = jnp.dot(applied_rows, value_cols, preferred_element_type=jnp.float32).astype(
            jnp.bfloat16
        )
        return jnp.einsum(
            "ay,sab->syb",
            spline,
            back_plane.reshape(slot_count, NB, -1),
            preferred_element_type=jnp.float32,
        ).astype(jnp.bfloat16)

    piece_of_place = jnp.sum(
        jnp.where(place_hot, jnp.arange(slot_count, dtype=jnp.int32)[None, :], 0), axis=1
    )

    def send_gradient(gradient_piece):
        send = jnp.take(gradient_piece, piece_of_place, axis=0, mode="clip")
        send = send.reshape(domain_count, capacity * NB, send.shape[-1])
        got = lax.all_to_all(send, "dom", split_axis=0, concat_axis=0, tiled=True)
        return got.reshape(domain_count * capacity, NB, -1)

    y_value_a = y_pass(spline, blips_a)
    y_curve_a = y_pass(second, blips_a)
    applied_a, values_low_a = plane_terms(
        y_value_a,
        y_curve_a,
        plane_value[:half, :half],
        plane_curve[:half, :half],
        window[:, :, :half],
    )
    gradient_a = gradient_of(applied_a, plane_value[:half, :early])
    got_grad_a = send_gradient(gradient_a)
    y_value = jnp.concatenate([y_value_a, y_pass(spline, blips_b)], axis=2)
    y_curve = jnp.concatenate([y_curve_a, y_pass(second, blips_b)], axis=2)
    applied_b, values_low_b = plane_terms(
        y_value, y_curve, plane_value[:, early:], plane_curve[:, early:], window[:, :, early:]
    )
    applied_rows = jnp.concatenate([applied_a[:, :early], applied_b], axis=1)
    gradient_b = gradient_of(applied_rows, plane_value[:, early:])
    got_grad_b = send_gradient(gradient_b)


    def overlap(values_low, applied):
        return lax.dot_general(
            values_low.reshape(slot_count, NB, -1),
            applied.reshape(slot_count, NB, -1),
            (((1, 2), (1, 2)), ((), ())),
            preferred_element_type=jnp.float32,
        )

    intersection = (
        overlap(values_low_a[:, :early], applied_a[:, :early]) + overlap(values_low_b, applied_b)
    ) / float(cell_count)
    select_full = (target[:, None] == jnp.arange(group_size, dtype=jnp.int32)[None, :]).astype(
        jnp.float32
    )
    weighted = jnp.dot(intersection, select_full, precision=lax.Precision.HIGHEST)
    send_ham = jnp.dot(
        place_hot.astype(jnp.float32), weighted, precision=lax.Precision.HIGHEST
    ).reshape(domain_count, capacity, group_size)
    shared_ham = lax.all_gather(send_ham, "dom", axis=0, tiled=True).reshape(
        domain_count, domain_count, capacity, group_size
    )
    row_hot = asked_of_me[None, :] == jnp.arange(owned_count, dtype=jnp.int32)[:, None]
    mine = lax.axis_index("dom") == jnp.arange(domain_count, dtype=jnp.int32)
    pick_ham = (
        row_hot.reshape(owned_count, domain_count, 1, capacity) & mine[None, None, :, None]
    ).astype(jnp.float32)
    hamilton = jnp.dot(
        pick_ham.reshape(owned_count, -1),
        shared_ham.reshape(-1, group_size),
        precision=lax.Precision.HIGHEST,
    )
    row_low = row_hot.astype(jnp.bfloat16)
    gradient = jnp.concatenate(
        [
            jnp.einsum("rs,syc->ryc", row_low, got, preferred_element_type=jnp.float32)
            for got in (got_grad_a, got_grad_b)
        ],
        axis=2,
    ).reshape(owned_count, cell_count)
    return (gradient, hamilton)


def solution(mesh):
    placed = (
        P(("grp", "dom"), None),
        P("dom", "grp", None),
        P(("grp", "dom"), None),
        P(("grp", "dom")),
        P(("grp", "dom")),
    )
    return jax.shard_map(
        on_device,
        mesh=mesh,
        in_specs=placed,
        out_specs=(P(("grp", "dom"), None), P(("grp", "dom"), None)),
        check_vma=False,
    )
```
